1024 devices in a mesh: pair: 64 (over z, core), narrow: 16 (over y, x).
Axes of the slice: x: 4, y: 4, z: 32, core: 2. Of those that a mesh axis runs over, the one named last changes fastest.
Arguments:
- trial_slab: bfloat16 [8, 2048, 10240], P(None, 'pair', 'narrow'), may hold values from -6 to 6
- ladder: bfloat16 [65536, 10240], P('pair', 'narrow'), may hold values from -0.0625 to 0.0625
- range_irreps: int32 [64], replicated, may hold values from 0 to 7, as said below
Outputs:
- sigma: bfloat16 [2048, 65536], P(('pair', 'narrow'))
The draws below stay inside these ranges and needn't reach their ends.
Inputs may be any that keep to these rules, and one draw needn't show every extreme that they name: `range_irreps`: non-decreasing along the pair index; the first entry is 0 and the last is 7.
All inputs are finite; a program needn't handle non-finite values.
Results may differ from the reference program's by a relative error of at most 0.019.
Values may be sent and summed in bfloat16 or wider, within the bound.
No kernel may reach another device: no remote copies, remote signals or barrier semaphores. Data moves between devices by JAX's collectives and lax.ppermute only.
A program may use at most 32 MiB of HBM per device.

```python
import jax
import jax.numpy as jnp
from jax import lax

CD = 10240
IRREPS = 8
AB_DEV = 1024
AB = 65536
ROWS = 2048
N_PAIR = 64
N_NARROW = 16


def draw_range_irreps(key, part):
    inner = jax.random.randint(key, (N_PAIR - 2,), 0, IRREPS).astype(jnp.int32)
    first = jnp.zeros((1,), jnp.int32)
    last = jnp.full((1,), IRREPS - 1, jnp.int32)
    return jnp.sort(jnp.concatenate([first, inner, last]))


def steps_of(key, shape, shards, smallest, top_value):
    factor_of, own = 1.0, jax.random.fold_in(key, 6)
    for axis_at, blocks in shards:
        heights = jnp.exp(jax.random.uniform(jax.random.fold_in(own, axis_at), (blocks,), jnp.float32, smallest / len(shards), top_value / len(shards)))
        factor_of = factor_of * jnp.repeat(heights, shape[axis_at] // blocks).reshape([-1 if axis == axis_at else 1 for axis in range(len(shape))])
    return factor_of


def gaussian(rng, shape, deviation, reach, split=(), kind=jnp.bfloat16):
    loudness = steps_of(rng, shape, split, -0.22, 0.18) if split else 1.0
    array = jax.random.normal(rng, shape, jnp.float32) * deviation * loudness
    return jnp.minimum(jnp.maximum(array, -reach), reach).astype(kind)


def setup_inputs(seed: int = 0) -> dict:
    key_list = jax.random.split(jax.random.key(seed), 4)
    trial_slab = gaussian(key_list[0], (IRREPS, ROWS, CD), 1.0, 6.0, ((1, 64), (2, 16)))
    ladder = gaussian(key_list[1], (AB, CD), CD ** -0.5, 0.0625, ((0, 64), (1, 16)))
    range_irreps = draw_range_irreps(jax.random.fold_in(key_list[3], 71), 0)
    return dict(trial_slab=trial_slab, ladder=ladder, range_irreps=range_irreps)


def reference(trial_slab, ladder, range_irreps):
    block = CD // N_NARROW
    ranges = ladder.reshape(N_PAIR, AB_DEV, N_NARROW, block)

    def one_range(inputs):
        weights, label = inputs
        slab = lax.dynamic_index_in_dim(trial_slab, label, 0, keepdims=False)
        slab = slab.reshape(ROWS, N_NARROW, block).astype(jnp.float32)
        partial_value = jnp.einsum("rnc,anc->nra", slab, weights.astype(jnp.float32))
        rounded = lax.optimization_barrier(partial_value.astype(jnp.bfloat16)).astype(jnp.float32)
        return jnp.sum(rounded, axis=0).astype(jnp.bfloat16)

    pieces = lax.map(one_range, (ranges, range_irreps))
    return jnp.transpose(pieces, (1, 0, 2)).reshape(ROWS, AB)
```

```python
import jax
import jax.numpy as jnp
from jax import lax
from jax.sharding import Mesh
from jax.sharding import PartitionSpec as P


def body(trial_slab, ladder, range_irreps):
    chips = lax.axis_size("z")
    cores = lax.axis_size("core")
    narrow_count = lax.axis_size("narrow")
    pair_count = chips * cores
    rows_out = trial_slab.shape[1] // narrow_count
    local_rows = trial_slab.shape[1]
    local_pairs = ladder.shape[0]
    core = lax.axis_index("core")
    me = lax.axis_index("z") * cores + core
    partner = me + 1 - 2 * core
    gathered = lax.all_gather(trial_slab, "z", axis=0, tiled=False)
    mine = jnp.take(gathered, range_irreps[me], axis=1)
    theirs = jnp.take(gathered, range_irreps[partner], axis=1)
    received = lax.ppermute(theirs, "core", [(0, 1), (1, 0)])
    low = jnp.where(core == 0, mine, received)
    high = jnp.where(core == 0, received, mine)
    arrived = jnp.stack([low, high], axis=1).reshape(pair_count, local_rows, -1)
    products = jnp.einsum("pmc,ac->mpa", arrived, ladder, preferred_element_type=jnp.float32)
    summed = lax.psum_scatter(
        products.reshape(-1, local_pairs).astype(jnp.bfloat16),
        "narrow",
        scatter_dimension=0,
        tiled=True,
    )
    rounded = summed.reshape(rows_out, pair_count, local_pairs)
    owned = lax.all_to_all(rounded, ("z", "core"), split_axis=1, concat_axis=1, tiled=True)
    return owned.reshape(rows_out, pair_count * local_pairs)


def solution(mesh):
    pair_count = mesh.shape["pair"]
    narrow_count = mesh.shape["narrow"]
    split = Mesh(mesh.devices.reshape(pair_count // 2, 2, narrow_count), ("z", "core", "narrow"))
    placed = (P(None, ("z", "core"), "narrow"), P(("z", "core"), "narrow"), P())
    return jax.shard_map(
        body, mesh=split, in_specs=placed, out_specs=P(("z", "core", "narrow"), None), check_vma=False
    )
```

```python
import jax
import jax.numpy as jnp
from jax import lax
from jax.sharding import Mesh
from jax.sharding import PartitionSpec as P


def body(trial_slab, ladder, range_irreps):
    chips = lax.axis_size("z")
    cores = lax.axis_size("core")
    narrow_count = lax.axis_size("narrow")
    pair_count = chips * cores
    irreps, local_rows, block = trial_slab.shape
    per_owner = local_rows // narrow_count
    local_pairs = ladder.shape[0]
    core = lax.axis_index("core")
    me = lax.axis_index("z") * cores + core
    partner = me + 1 - 2 * core
    slab = trial_slab.reshape(irreps, narrow_count, per_owner, block)
    pieces = []
    for j in range(per_owner):
        gathered = lax.all_gather(slab[:, :, j, :], "z", axis=0, tiled=False)
        mine = jnp.take(gathered, range_irreps[me], axis=1)
        theirs = jnp.take(gathered, range_irreps[partner], axis=1)
        received = lax.ppermute(theirs, "core", [(0, 1), (1, 0)])
        low = jnp.where(core == 0, mine, received)
        high = jnp.where(core == 0, received, mine)
        arrived = jnp.stack([low, high], axis=1).reshape(pair_count, narrow_count, block)
        products = jnp.einsum("poc,ac->opa", arrived, ladder, preferred_element_type=jnp.float32)
        exchanged = lax.all_to_all(
            products.astype(jnp.bfloat16), "narrow", split_axis=0, concat_axis=0, tiled=True
        )
        summed = jnp.sum(exchanged.astype(jnp.float32), axis=0).astype(jnp.bfloat16)
        owned = lax.all_to_all(summed, ("z", "core"), split_axis=0, concat_axis=0, tiled=True)
        pieces.append(owned.reshape(pair_count * local_pairs))
    return jnp.stack(pieces, axis=0)


def solution(mesh):
    pair_count = mesh.shape["pair"]
    narrow_count = mesh.shape["narrow"]
    split = Mesh(mesh.devices.reshape(pair_count // 2, 2, narrow_count), ("z", "core", "narrow"))
    placed = (P(None, ("z", "core"), "narrow"), P(("z", "core"), "narrow"), P())
    return jax.shard_map(
        body, mesh=split, in_specs=placed, out_specs=P(("z", "core", "narrow"), None), check_vma=False
    )
```

```python
import jax
import jax.numpy as jnp
from jax import lax
from jax.sharding import Mesh
from jax.sharding import PartitionSpec as P


def body(trial_slab, ladder, range_irreps):
    chips = lax.axis_size("z")
    cores = lax.axis_size("core")
    narrow_count = lax.axis_size("narrow")
    pair_count = chips * cores
    irreps, local_rows, block = trial_slab.shape
    per_owner = local_rows // narrow_count
    local_pairs = ladder.shape[0]
    core = lax.axis_index("core")
    me = lax.axis_index("z") * cores + core
    partner = me + 1 - 2 * core
    gathered = lax.all_gather(trial_slab, "z", axis=0, tiled=False)
    mine = jnp.take(gathered, range_irreps[me], axis=1)
    theirs = jnp.take(gathered, range_irreps[partner], axis=1)
    received = lax.ppermute(theirs, "core", [(0, 1), (1, 0)])
    low = jnp.where(core == 0, mine, received)
    high = jnp.where(core == 0, received, mine)
    arrived = jnp.stack([low, high], axis=1).reshape(pair_count, narrow_count, per_owner, block)
    pieces = []
    for j in range(per_owner):
        products = jnp.einsum(
            "poc,ac->opa", arrived[:, :, j, :], ladder, preferred_element_type=jnp.float32
        )
        exchanged = lax.all_to_all(
            products.astype(jnp.bfloat16), "narrow", split_axis=0, concat_axis=0, tiled=True
        )
        summed = jnp.sum(exchanged.astype(jnp.float32), axis=0).astype(jnp.bfloat16)
        owned = lax.all_to_all(summed, ("z", "core"), split_axis=0, concat_axis=0, tiled=True)
        pieces.append(owned.reshape(pair_count * local_pairs))
    return jnp.stack(pieces, axis=0)


def solution(mesh):
    pair_count = mesh.shape["pair"]
    narrow_count = mesh.shape["narrow"]
    split = Mesh(mesh.devices.reshape(pair_count // 2, 2, narrow_count), ("z", "core", "narrow"))
    placed = (P(None, ("z", "core"), "narrow"), P(("z", "core"), "narrow"), P())
    return jax.shard_map(
        body, mesh=split, in_specs=placed, out_specs=P(("z", "core", "narrow"), None), check_vma=False
    )
```

```python
import jax
import jax.numpy as jnp
from jax import lax
from jax.sharding import Mesh
from jax.sharding import PartitionSpec as P

Z_HI = 4


def body(trial_slab, ladder, range_irreps):
    z_lo_count = lax.axis_size("z_lo")
    chips = lax.axis_size("z_hi") * z_lo_count
    cores = lax.axis_size("core")
    narrow_count = lax.axis_size("narrow")
    pair_count = chips * cores
    irreps, local_rows, block = trial_slab.shape
    per_owner = local_rows // narrow_count
    local_pairs = ladder.shape[0]
    core = lax.axis_index("core")
    chip = lax.axis_index("z_hi") * z_lo_count + lax.axis_index("z_lo")
    me = chip * cores + core
    partner = me + 1 - 2 * core
    near = lax.all_gather(trial_slab, "z_lo", axis=0, tiled=True)
    gathered = lax.all_gather(near, "z_hi", axis=0, tiled=True).reshape(chips, irreps, local_rows, block)
    mine = jnp.take(gathered, range_irreps[me], axis=1)
    theirs = jnp.take(gathered, range_irreps[partner], axis=1)
    received = lax.ppermute(theirs, "core", [(0, 1), (1, 0)])
    products = jnp.stack(
        [
            jnp.einsum("zmc,ac->mza", rows, ladder, preferred_element_type=jnp.float32)
            for rows in (mine, received)
        ],
        axis=1,
    )
    partial = products.astype(jnp.bfloat16).reshape(narrow_count, per_owner, cores, chips, local_pairs)
    exchanged = lax.all_to_all(partial, "narrow", split_axis=0, concat_axis=0, tiled=True)
    summed = jnp.sum(exchanged.astype(jnp.float32), axis=0).astype(jnp.bfloat16)
    by_core = jnp.where(core == 0, summed, summed[:, ::-1])
    by_device = jnp.transpose(by_core, (0, 2, 1, 3)).reshape(per_owner, pair_count, local_pairs)
    owned = lax.all_to_all(by_device, ("z_hi", "z_lo", "core"), split_axis=1, concat_axis=1, tiled=True)
    return owned.reshape(per_owner, pair_count * local_pairs)


def solution(mesh):
    pair_count = mesh.shape["pair"]
    narrow_count = mesh.shape["narrow"]
    devices = mesh.devices.reshape(Z_HI, pair_count // (2 * Z_HI), 2, narrow_count)
    split = Mesh(devices, ("z_hi", "z_lo", "core", "narrow"))
    pair = ("z_hi", "z_lo", "core")
    placed = (P(None, pair, "narrow"), P(pair, "narrow"), P())
    return jax.shard_map(
        body, mesh=split, in_specs=placed, out_specs=P(pair + ("narrow",), None), check_vma=False
    )
```

```python
import jax
import jax.numpy as jnp
from jax import lax
from jax.sharding import Mesh
from jax.sharding import PartitionSpec as P


def body(trial_slab, ladder, range_irreps):
    chips = lax.axis_size("z")
    cores = lax.axis_size("core")
    narrow_count = lax.axis_size("narrow")
    pair_count = chips * cores
    irreps, local_rows, block = trial_slab.shape
    per_owner = local_rows // narrow_count
    local_pairs = ladder.shape[0]
    core = lax.axis_index("core")
    me = lax.axis_index("z") * cores + core
    partner = me + 1 - 2 * core
    gathered = lax.all_gather(trial_slab, "z", axis=0, tiled=False)
    mine = jnp.take(gathered, range_irreps[me], axis=1)
    theirs = jnp.take(gathered, range_irreps[partner], axis=1)
    received = lax.ppermute(theirs, "core", [(0, 1), (1, 0)])
    low = jnp.where(core == 0, mine, received)
    high = jnp.where(core == 0, received, mine)
    arrived = jnp.stack([low, high], axis=1).reshape(pair_count, narrow_count, per_owner, block)
    products = jnp.einsum("pojc,ac->jopa", arrived, ladder, preferred_element_type=jnp.float32)
    partial = products.astype(jnp.bfloat16)
    sums = []
    for j in range(per_owner):
        exchanged = lax.all_to_all(partial[j], "narrow", split_axis=0, concat_axis=0, tiled=True)
        sums.append(jnp.sum(exchanged.astype(jnp.float32), axis=0).astype(jnp.bfloat16))
    summed = jnp.stack(sums, axis=0)
    owned = lax.all_to_all(summed, ("z", "core"), split_axis=1, concat_axis=1, tiled=True)
    return owned.reshape(per_owner, pair_count * local_pairs)


def solution(mesh):
    pair_count = mesh.shape["pair"]
    narrow_count = mesh.shape["narrow"]
    split = Mesh(mesh.devices.reshape(pair_count // 2, 2, narrow_count), ("z", "core", "narrow"))
    placed = (P(None, ("z", "core"), "narrow"), P(("z", "core"), "narrow"), P())
    return jax.shard_map(
        body, mesh=split, in_specs=placed, out_specs=P(("z", "core", "narrow"), None), check_vma=False
    )
```

```python
import jax
import jax.numpy as jnp
from jax import lax
from jax.sharding import Mesh
from jax.sharding import PartitionSpec as P

GROUPS = 4


def body(trial_slab, ladder, range_irreps):
    chips = lax.axis_size("z")
    cores = lax.axis_size("core")
    narrow_count = lax.axis_size("narrow")
    pair_count = chips * cores
    irreps, local_rows, block = trial_slab.shape
    per_owner = local_rows // narrow_count
    local_pairs = ladder.shape[0]
    core = lax.axis_index("core")
    chip = lax.axis_index("z")
    me = chip * cores + core
    partner = me + 1 - 2 * core
    mine_irrep = range_irreps[me]
    partner_irrep = range_irreps[partner]
    up = [(i, (i + 1) % chips) for i in range(chips)]
    down = [(i, (i - 1) % chips) for i in range(chips)]

    arrivals = [(0, trial_slab)]
    going_up = going_down = trial_slab
    for distance in range(1, chips // 2 + 1):
        going_up = lax.ppermute(going_up, "z", up)
        arrivals.append((chips - distance, going_up))
        if distance < chips - distance:
            going_down = lax.ppermute(going_down, "z", down)
            arrivals.append((distance, going_down))

    size = -(-len(arrivals) // GROUPS)
    order, sums = [], []
    for start in range(0, len(arrivals), size):
        group = arrivals[start:start + size]
        order += [r for r, _ in group]
        mine = jnp.stack([jnp.take(b, mine_irrep, axis=0) for _, b in group])
        theirs = jnp.stack([jnp.take(b, partner_irrep, axis=0) for _, b in group])
        received = lax.ppermute(theirs, "core", [(0, 1), (1, 0)])
        rows = jnp.stack([mine, received])
        products = jnp.einsum("snmc,ac->msna", rows, ladder, preferred_element_type=jnp.float32)
        partial = products.astype(jnp.bfloat16).reshape(
            narrow_count, per_owner, cores, len(group), local_pairs
        )
        exchanged = lax.all_to_all(partial, "narrow", split_axis=0, concat_axis=0, tiled=True)
        sums.append(jnp.sum(exchanged.astype(jnp.float32), axis=0).astype(jnp.bfloat16))
    summed = jnp.concatenate(sums, axis=2)
    by_offset = jnp.take(summed, jnp.array([order.index(r) for r in range(chips)]), axis=2)
    by_chip = jnp.roll(by_offset, chip, axis=2)
    by_core = jnp.where(core == 0, by_chip, by_chip[:, ::-1])
    by_device = jnp.transpose(by_core, (0, 2, 1, 3)).reshape(per_owner, pair_count, local_pairs)
    owned = lax.all_to_all(by_device, ("z", "core"), split_axis=1, concat_axis=1, tiled=True)
    return owned.reshape(per_owner, pair_count * local_pairs)


def solution(mesh):
    pair_count = mesh.shape["pair"]
    narrow_count = mesh.shape["narrow"]
    split = Mesh(mesh.devices.reshape(pair_count // 2, 2, narrow_count), ("z", "core", "narrow"))
    placed = (P(None, ("z", "core"), "narrow"), P(("z", "core"), "narrow"), P())
    return jax.shard_map(
        body, mesh=split, in_specs=placed, out_specs=P(("z", "core", "narrow"), None), check_vma=False
    )
```

```python
import jax
import jax.numpy as jnp
from jax import lax
from jax.sharding import Mesh
from jax.sharding import PartitionSpec as P

GROUPS = 4


def body(trial_slab, ladder, range_irreps):
    chips = lax.axis_size("z")
    cores = lax.axis_size("core")
    narrow_count = lax.axis_size("narrow")
    pair_count = chips * cores
    irreps, local_rows, block = trial_slab.shape
    per_owner = local_rows // narrow_count
    local_pairs = ladder.shape[0]
    core = lax.axis_index("core")
    chip = lax.axis_index("z")
    me = chip * cores + core
    partner = me + 1 - 2 * core
    mine_irrep = range_irreps[me]
    partner_irrep = range_irreps[partner]
    up = [(i, (i + 1) % chips) for i in range(chips)]
    down = [(i, (i - 1) % chips) for i in range(chips)]

    arrivals = [(0, trial_slab)]
    going_up = going_down = trial_slab
    for distance in range(1, chips // 2 + 1):
        going_up = lax.ppermute(going_up, "z", up)
        arrivals.append((chips - distance, going_up))
        if distance < chips - distance:
            going_down = lax.ppermute(going_down, "z", down)
            arrivals.append((distance, going_down))

    size = -(-len(arrivals) // GROUPS)
    order, sums = [], []
    for start in range(0, len(arrivals), size):
        group = arrivals[start:start + size]
        order += [r for r, _ in group]
        blocks = jnp.stack([b for _, b in group])
        mine = jnp.take(blocks, mine_irrep, axis=1)
        theirs = jnp.take(blocks, partner_irrep, axis=1)
        received = lax.ppermute(theirs, "core", [(0, 1), (1, 0)])
        rows = jnp.stack([mine, received])
        products = jnp.einsum("snmc,ac->msna", rows, ladder, preferred_element_type=jnp.float32)
        partial = products.astype(jnp.bfloat16).reshape(
            narrow_count, per_owner, cores, len(group), local_pairs
        )
        exchanged = lax.all_to_all(partial, "narrow", split_axis=0, concat_axis=0, tiled=True)
        sums.append(jnp.sum(exchanged.astype(jnp.float32), axis=0).astype(jnp.bfloat16))
    summed = jnp.concatenate(sums, axis=2)
    by_offset = jnp.take(summed, jnp.array([order.index(r) for r in range(chips)]), axis=2)
    by_chip = jnp.roll(by_offset, chip, axis=2)
    by_core = jnp.where(core == 0, by_chip, by_chip[:, ::-1])
    by_device = jnp.transpose(by_core, (0, 2, 1, 3)).reshape(per_owner, pair_count, local_pairs)
    owned = lax.all_to_all(by_device, ("z", "core"), split_axis=1, concat_axis=1, tiled=True)
    return owned.reshape(per_owner, pair_count * local_pairs)


def solution(mesh):
    pair_count = mesh.shape["pair"]
    narrow_count = mesh.shape["narrow"]
    split = Mesh(mesh.devices.reshape(pair_count // 2, 2, narrow_count), ("z", "core", "narrow"))
    placed = (P(None, ("z", "core"), "narrow"), P(("z", "core"), "narrow"), P())
    return jax.shard_map(
        body, mesh=split, in_specs=placed, out_specs=P(("z", "core", "narrow"), None), check_vma=False
    )
```

```python
import jax
import jax.numpy as jnp
from jax import lax
from jax.sharding import Mesh
from jax.sharding import PartitionSpec as P

GROUPS = 4


def body(trial_slab, ladder, range_irreps):
    chips = lax.axis_size("z")
    cores = lax.axis_size("core")
    narrow_count = lax.axis_size("narrow")
    pair_count = chips * cores
    irreps, local_rows, block = trial_slab.shape
    per_owner = local_rows // narrow_count
    local_pairs = ladder.shape[0]
    core = lax.axis_index("core")
    chip = lax.axis_index("z")
    me = chip * cores + core
    partner = me + 1 - 2 * core
    mine_irrep = range_irreps[me]
    partner_irrep = range_irreps[partner]
    step = [
        (z * cores + c, ((z + 1 - 2 * c) % chips) * cores + c) for z in range(chips) for c in range(cores)
    ]

    arrivals = [(0, trial_slab)]
    going = trial_slab
    for distance in range(1, chips):
        going = lax.ppermute(going, ("z", "core"), step)
        arrivals.append((distance, going))

    size = -(-len(arrivals) // GROUPS)
    order, sums = [], []
    for start in range(0, len(arrivals), size):
        group = arrivals[start:start + size]
        order += [r for r, _ in group]
        mine = jnp.stack([jnp.take(b, mine_irrep, axis=0) for _, b in group])
        theirs = jnp.stack([jnp.take(b, partner_irrep, axis=0) for _, b in group])
        received = lax.ppermute(theirs, "core", [(0, 1), (1, 0)])
        rows = jnp.stack([mine, received])
        products = jnp.einsum("snmc,ac->msna", rows, ladder, preferred_element_type=jnp.float32)
        partial = products.astype(jnp.bfloat16).reshape(
            narrow_count, per_owner, cores, len(group), local_pairs
        )
        exchanged = lax.all_to_all(partial, "narrow", split_axis=0, concat_axis=0, tiled=True)
        sums.append(jnp.sum(exchanged.astype(jnp.float32), axis=0).astype(jnp.bfloat16))
    summed = jnp.concatenate(sums, axis=2)
    by_distance = jnp.take(summed, jnp.array([order.index(d) for d in range(chips)]), axis=2)
    by_core = jnp.where(core == 0, by_distance, by_distance[:, ::-1])
    from_below = jnp.take(by_core[:, 0], jnp.array([(-d) % chips for d in range(chips)]), axis=1)
    by_chip = jnp.stack(
        [jnp.roll(from_below, chip, axis=1), jnp.roll(by_core[:, 1], chip, axis=1)], axis=1
    )
    by_device = jnp.transpose(by_chip, (0, 2, 1, 3)).reshape(per_owner, pair_count, local_pairs)
    owned = lax.all_to_all(by_device, ("z", "core"), split_axis=1, concat_axis=1, tiled=True)
    return owned.reshape(per_owner, pair_count * local_pairs)


def solution(mesh):
    pair_count = mesh.shape["pair"]
    narrow_count = mesh.shape["narrow"]
    split = Mesh(mesh.devices.reshape(pair_count // 2, 2, narrow_count), ("z", "core", "narrow"))
    placed = (P(None, ("z", "core"), "narrow"), P(("z", "core"), "narrow"), P())
    return jax.shard_map(
        body, mesh=split, in_specs=placed, out_specs=P(("z", "core", "narrow"), None), check_vma=False
    )
```

```python
import jax
import jax.numpy as jnp
from jax import lax
from jax.sharding import Mesh
from jax.sharding import PartitionSpec as P

GROUPS = 4


def body(trial_slab, ladder, range_irreps):
    chips = lax.axis_size("z")
    cores = lax.axis_size("core")
    narrow_count = lax.axis_size("narrow")
    pair_count = chips * cores
    irreps, local_rows, block = trial_slab.shape
    per_owner = local_rows // narrow_count
    local_pairs = ladder.shape[0]
    core = lax.axis_index("core")
    chip = lax.axis_index("z")
    me = chip * cores + core
    partner = me + 1 - 2 * core
    mine_irrep = range_irreps[me]
    partner_irrep = range_irreps[partner]
    up = [(i, (i + 1) % chips) for i in range(chips)]
    down = [(i, (i - 1) % chips) for i in range(chips)]

    halves = tuple(jnp.split(trial_slab, 2, axis=1))
    arrivals = [(0, halves)]
    going_up = going_down = halves
    for distance in range(1, chips // 2 + 1):
        going_up = tuple(lax.ppermute(h, "z", up) for h in going_up)
        arrivals.append((chips - distance, going_up))
        if distance < chips - distance:
            going_down = tuple(lax.ppermute(h, "z", down) for h in going_down)
            arrivals.append((distance, going_down))

    size = -(-len(arrivals) // GROUPS)
    order, sums = [], []
    for start in range(0, len(arrivals), size):
        group = arrivals[start:start + size]
        order += [r for r, _ in group]
        mine = jnp.stack([jnp.concatenate([jnp.take(h, mine_irrep, axis=0) for h in b]) for _, b in group])
        theirs = jnp.stack(
            [jnp.concatenate([jnp.take(h, partner_irrep, axis=0) for h in b]) for _, b in group]
        )
        received = lax.ppermute(theirs, "core", [(0, 1), (1, 0)])
        rows = jnp.stack([mine, received])
        products = jnp.einsum("snmc,ac->msna", rows, ladder, preferred_element_type=jnp.float32)
        partial = products.astype(jnp.bfloat16).reshape(
            narrow_count, per_owner, cores, len(group), local_pairs
        )
        exchanged = lax.all_to_all(partial, "narrow", split_axis=0, concat_axis=0, tiled=True)
        sums.append(jnp.sum(exchanged.astype(jnp.float32), axis=0).astype(jnp.bfloat16))
    summed = jnp.concatenate(sums, axis=2)
    by_offset = jnp.take(summed, jnp.array([order.index(r) for r in range(chips)]), axis=2)
    by_chip = jnp.roll(by_offset, chip, axis=2)
    by_core = jnp.where(core == 0, by_chip, by_chip[:, ::-1])
    by_device = jnp.transpose(by_core, (0, 2, 1, 3)).reshape(per_owner, pair_count, local_pairs)
    owned = lax.all_to_all(by_device, ("z", "core"), split_axis=1, concat_axis=1, tiled=True)
    return owned.reshape(per_owner, pair_count * local_pairs)


def solution(mesh):
    pair_count = mesh.shape["pair"]
    narrow_count = mesh.shape["narrow"]
    split = Mesh(mesh.devices.reshape(pair_count // 2, 2, narrow_count), ("z", "core", "narrow"))
    placed = (P(None, ("z", "core"), "narrow"), P(("z", "core"), "narrow"), P())
    return jax.shard_map(
        body, mesh=split, in_specs=placed, out_specs=P(("z", "core", "narrow"), None), check_vma=False
    )
```

```python
import jax
import jax.numpy as jnp
from jax import lax
from jax.sharding import Mesh
from jax.sharding import PartitionSpec as P

def body(trial_slab, ladder, range_irreps):
    chips = lax.axis_size("z")
    cores = lax.axis_size("core")
    narrow_count = lax.axis_size("narrow")
    pair_count = chips * cores
    irreps, local_rows, block = trial_slab.shape
    per_owner = local_rows // narrow_count
    local_pairs = ladder.shape[0]
    core = lax.axis_index("core")
    chip = lax.axis_index("z")
    me = chip * cores + core
    partner = me + 1 - 2 * core
    mine_irrep = range_irreps[me]
    partner_irrep = range_irreps[partner]
    up = [(i, (i + 1) % chips) for i in range(chips)]
    down = [(i, (i - 1) % chips) for i in range(chips)]

    arrivals = [(0, trial_slab)]
    going_up = going_down = trial_slab
    for distance in range(1, chips // 2 + 1):
        going_up = lax.ppermute(going_up, "z", up)
        arrivals.append((chips - distance, going_up))
        if distance < chips - distance:
            going_down = lax.ppermute(going_down, "z", down)
            arrivals.append((distance, going_down))

    bounds = [0, 10, 20, 28, len(arrivals)]
    order, sums = [], []
    for start, end in zip(bounds[:-1], bounds[1:]):
        group = arrivals[start:end]
        order += [r for r, _ in group]
        mine = jnp.stack([jnp.take(b, mine_irrep, axis=0) for _, b in group])
        theirs = jnp.stack([jnp.take(b, partner_irrep, axis=0) for _, b in group])
        received = lax.ppermute(theirs, "core", [(0, 1), (1, 0)])
        rows = jnp.stack([mine, received])
        products = jnp.einsum("snmc,ac->msna", rows, ladder, preferred_element_type=jnp.float32)
        partial = products.astype(jnp.bfloat16).reshape(
            narrow_count, per_owner, cores, len(group), local_pairs
        )
        exchanged = lax.all_to_all(partial, "narrow", split_axis=0, concat_axis=0, tiled=True)
        sums.append(jnp.sum(exchanged.astype(jnp.float32), axis=0).astype(jnp.bfloat16))
    summed = jnp.concatenate(sums, axis=2)
    by_offset = jnp.take(summed, jnp.array([order.index(r) for r in range(chips)]), axis=2)
    by_chip = jnp.roll(by_offset, chip, axis=2)
    by_core = jnp.where(core == 0, by_chip, by_chip[:, ::-1])
    by_device = jnp.transpose(by_core, (0, 2, 1, 3)).reshape(per_owner, pair_count, local_pairs)
    owned = lax.all_to_all(by_device, ("z", "core"), split_axis=1, concat_axis=1, tiled=True)
    return owned.reshape(per_owner, pair_count * local_pairs)


def solution(mesh):
    pair_count = mesh.shape["pair"]
    narrow_count = mesh.shape["narrow"]
    split = Mesh(mesh.devices.reshape(pair_count // 2, 2, narrow_count), ("z", "core", "narrow"))
    placed = (P(None, ("z", "core"), "narrow"), P(("z", "core"), "narrow"), P())
    return jax.shard_map(
        body, mesh=split, in_specs=placed, out_specs=P(("z", "core", "narrow"), None), check_vma=False
    )
```
